512 devices in a mesh: ind: 64 (over y, z), snp: 8 (over x, core).
Axes of the slice: x: 4, y: 8, z: 8, core: 2. Of those that a mesh axis runs over, the one named last changes fastest.
Arguments:
- genotypes: int32 [4096, 16384], P('ind', 'snp'), may hold values from 0 to 2
- observed: int32 [4096, 16384], P('ind', 'snp'), may hold values from 0 to 1
- ancestry: float32 [4096, 32], P('ind'), may hold values from 0.018 to 54.6, as said below
- freqs: float32 [16384, 32], P(('snp', 'ind')), may hold values from 0.05 to 0.95
Outputs:
- ancestry_out: float32 [4096, 32], P('ind')
- freqs_out: float32 [16384, 32], P(('snp', 'ind'))
The draws below stay inside these ranges and needn't reach their ends.
Inputs may be any that keep to these rules, and one draw needn't show every extreme that they name: `ancestry`: positive weights.
All inputs are finite; a program needn't handle non-finite values.
Results may differ from the reference program's by a relative error of at most 0.0003.
Values sent between devices are 32-bit elements; how exact they have to be, the bound alone decides.
No kernel may reach another device: no remote copies, remote signals or barrier semaphores. Data moves between devices by JAX's collectives and lax.ppermute only.
A program may use at most 64 MiB of HBM per device.

```python
import jax
import jax.numpy as jnp
from jax import lax

K = 32
ND = 64
STEPS = 3
N = 4096
M = 16384


def draw_observed(key, part):
    rows = jnp.arange(N, dtype=jnp.int32)[:, None]
    rate = 30 + 65 * rows // (N - 1)
    roll = jax.random.randint(jax.random.fold_in(key, 11), (N, M), 0, 100, dtype=jnp.int32)
    return (roll < rate).astype(jnp.int32)


def draw_ancestry(key, part):
    spread = 0.5 + 3.5 * jnp.arange(N, dtype=jnp.float32)[:, None] / (N - 1)
    inner = jax.random.fold_in(key, 23)
    unit = jnp.clip(0.5 * jax.random.normal(inner, (N, K), jnp.float32), -1.0, 1.0)
    return jnp.exp(unit * spread).astype(jnp.float32)


def set_ends(array, key, smallest, top_value):
    extent = array.shape
    spot = [jax.random.randint(jax.random.fold_in(key, axis), (), 0, extent[axis]) for axis in range(len(extent))]
    array = array.at[tuple(spot)].set(smallest)
    longest = extent.index(max(extent))
    spot[longest] = (spot[longest] + 1) % extent[longest]
    return array.at[tuple(spot)].set(top_value)


def level_of(rng, extent, shards, smallest, high):
    def one(position, parts):
        heights = jax.random.uniform(jax.random.fold_in(jax.random.fold_in(rng, 6), position), (parts,), jnp.float32, smallest / len(shards), high / len(shards))
        return jnp.repeat(jnp.exp(heights), extent[position] // parts).reshape((-1,) + (1,) * (len(extent) - position - 1))

    level = one(*shards[0])
    for cut in shards[1:]:
        level = level * one(*cut)
    return level


def setup_inputs(seed: int = 0) -> dict:
    keys = jax.random.split(jax.random.key(seed), 5)
    return {
        "genotypes": set_ends(jax.random.randint(keys[0], (N, M), 0, 3), jax.random.fold_in(keys[0], 1), 0, 2).astype(jnp.int32),
        "observed": draw_observed(jax.random.fold_in(keys[4], 71), 0),
        "ancestry": draw_ancestry(jax.random.fold_in(keys[4], 71), 0),
        "freqs": jnp.clip(0.05 + 0.9 * jax.random.uniform(keys[3], (M, K), jnp.float32) ** level_of(keys[3], (M, K), ((0, 512),), -0.2, 0.2), 0.05, 0.95),
    }


clip_low = 1e-05
high = lax.Precision.HIGHEST

def em_map(hits, misses, q, f):
    blocks = q.shape[0] // ND
    width = f.shape[0]
    hit_blocks = hits.reshape(blocks, ND, width)
    miss_blocks = misses.reshape(blocks, ND, width)
    q_blocks = q.reshape(blocks, ND, q.shape[1])

    def one_block(carry, items):
        hit_rows, miss_rows, q_rows = items
        prob = jnp.dot(q_rows, f.T, precision=high, preferred_element_type=jnp.float32)
        ratio_a = hit_rows / prob
        ratio_b = miss_rows / (1.0 - prob)
        sum_a = jnp.dot(ratio_a, f, precision=high, preferred_element_type=jnp.float32)
        sum_b = jnp.dot(ratio_b, 1.0 - f, precision=high, preferred_element_type=jnp.float32)
        q_next = q_rows * (sum_a + sum_b)
        q_next = q_next / lax.optimization_barrier(jnp.sum(q_next, axis=1, keepdims=True))
        c_part = jnp.dot(ratio_a.T, q_rows, precision=high, preferred_element_type=jnp.float32)
        d_part = jnp.dot(ratio_b.T, q_rows, precision=high, preferred_element_type=jnp.float32)
        return ((carry[0] + c_part, carry[1] + d_part), q_next)
    start = (jnp.zeros(f.shape, jnp.float32), jnp.zeros(f.shape, jnp.float32))
    (c_total, d_total), q_new = lax.scan(one_block, start, (hit_blocks, miss_blocks, q_blocks))
    f_new = f * c_total / (f * c_total + (1.0 - f) * d_total)
    return (q_new.reshape(q.shape), f_new)

def reference(genotypes, observed, ancestry, freqs):
    geno = genotypes.astype(jnp.float32)
    seen = observed.astype(jnp.float32)
    hits = seen * geno
    misses = seen * (2.0 - geno)
    q_zero = ancestry / lax.optimization_barrier(jnp.sum(ancestry, axis=1, keepdims=True))
    f_zero = freqs
    for step in range(STEPS):
        q_one, f_one = em_map(hits, misses, q_zero, f_zero)
        q_two, f_two = em_map(hits, misses, q_one, f_one)
        rq = q_one - q_zero
        rf = f_one - f_zero
        vq = q_two - 2.0 * q_one + q_zero
        vf = f_two - 2.0 * f_one + f_zero
        first = jnp.sum(rq * rq) + jnp.sum(rf * rf)
        second = jnp.sum(vq * vq) + jnp.sum(vf * vf)
        alpha = -jnp.sqrt(first / (second + 1e-20))
        q_ext = jnp.clip(q_zero - 2.0 * alpha * rq + alpha * alpha * vq, clip_low, 1.0 - clip_low)
        q_zero = q_ext / lax.optimization_barrier(jnp.sum(q_ext, axis=1, keepdims=True))
        f_zero = jnp.clip(f_zero - 2.0 * alpha * rf + alpha * alpha * vf, clip_low, 1.0 - clip_low)
    return (q_zero, f_zero)
```

```python
import jax
import jax.numpy as jnp
from jax import lax
from jax.sharding import Mesh
from jax.sharding import PartitionSpec as P

STEPS = 3


clip_low = 1e-05
high = lax.Precision.HIGHEST

IND_AXES = ("yh", "yl", "z")
SNP_AXES = ("x", "c")
ROW_GROUP = ("yl", "z")
COL_GROUP = ("c", "x", "yh")


def doubling_sum(value, axes):
    for name in axes:
        size = lax.axis_size(name)
        step = 1
        while step < size:
            pairs = [(j, j ^ step) for j in range(size)]
            value = value + lax.ppermute(value, name, pairs)
            step *= 2
    return value


def per_device(genotypes, observed, ancestry, freqs):
    quarter = lax.axis_size("yh")
    geno = genotypes.astype(jnp.float32)
    seen = observed.astype(jnp.float32)
    counts = jnp.stack([seen * geno, seen * (2.0 - geno)])
    counts = lax.all_to_all(counts, "yh", 2, 1, tiled=True)
    hits, misses = counts[0], counts[1]
    own_rows = ancestry.shape[0]
    own_snps = freqs.shape[0]
    q_own = ancestry / jnp.sum(ancestry, axis=1, keepdims=True)
    q_zero = lax.all_gather(q_own, "yh", axis=0, tiled=True)
    f_zero = lax.all_gather(freqs, ROW_GROUP, axis=0, tiled=True)

    def em_map(q_rows, f_state):
        prob = jnp.dot(q_rows, f_state.T, precision=high, preferred_element_type=jnp.float32)
        ratio_a = hits / prob
        ratio_b = misses / (1.0 - prob)
        sum_a = jnp.dot(ratio_a, f_state, precision=high, preferred_element_type=jnp.float32)
        sum_b = jnp.dot(ratio_b, 1.0 - f_state, precision=high, preferred_element_type=jnp.float32)
        c_part = lax.dot_general(
            ratio_a, q_rows, (((0,), (0,)), ((), ())), precision=high, preferred_element_type=jnp.float32
        )
        d_part = lax.dot_general(
            ratio_b, q_rows, (((0,), (0,)), ((), ())), precision=high, preferred_element_type=jnp.float32
        )
        q_sum = doubling_sum(sum_a + sum_b, COL_GROUP)
        cd_total = doubling_sum(jnp.concatenate([c_part, d_part], axis=1), ROW_GROUP)
        q_next = q_rows * q_sum
        q_next = q_next / jnp.sum(q_next, axis=1, keepdims=True)
        width = f_state.shape[1]
        c_total, d_total = cd_total[:, :width], cd_total[:, width:]
        f_next = f_state * c_total / (f_state * c_total + (1.0 - f_state) * d_total)
        return (q_next, f_next)

    for step in range(STEPS):
        q_one, f_one = em_map(q_zero, f_zero)
        q_two, f_two = em_map(q_one, f_one)
        rq = q_one - q_zero
        rf = f_one - f_zero
        vq = q_two - 2.0 * q_one + q_zero
        vf = f_two - 2.0 * f_one + f_zero
        q_parts = doubling_sum(jnp.stack([jnp.sum(rq * rq), jnp.sum(vq * vq)]), ROW_GROUP)
        f_parts = doubling_sum(jnp.stack([jnp.sum(rf * rf), jnp.sum(vf * vf)]), COL_GROUP)
        first = q_parts[0] + f_parts[0]
        second = q_parts[1] + f_parts[1]
        alpha = -jnp.sqrt(first / (second + 1e-20))
        q_ext = jnp.clip(q_zero - 2.0 * alpha * rq + alpha * alpha * vq, clip_low, 1.0 - clip_low)
        q_zero = q_ext / jnp.sum(q_ext, axis=1, keepdims=True)
        f_zero = jnp.clip(f_zero - 2.0 * alpha * rf + alpha * alpha * vf, clip_low, 1.0 - clip_low)
    q_final = lax.dynamic_slice_in_dim(q_zero, lax.axis_index("yh") * own_rows, own_rows, 0)
    f_index = lax.axis_index("yl") * lax.axis_size("z") + lax.axis_index("z")
    f_final = lax.dynamic_slice_in_dim(f_zero, f_index * own_snps, own_snps, 0)
    del quarter
    return (q_final, f_final)


def solution(mesh):
    ind_size = mesh.shape["ind"]
    snp_size = mesh.shape["snp"]
    quarter = 4
    lanes = ind_size // quarter
    view = Mesh(
        mesh.devices.reshape(quarter, 2, lanes // 2, snp_size // 2, 2),
        ("yh", "yl", "z", "x", "c"),
    )
    in_specs = (
        P(IND_AXES, SNP_AXES),
        P(IND_AXES, SNP_AXES),
        P(IND_AXES, None),
        P(SNP_AXES + IND_AXES, None),
    )
    out_specs = (P(IND_AXES, None), P(SNP_AXES + IND_AXES, None))
    return jax.shard_map(
        per_device, mesh=view, in_specs=in_specs, out_specs=out_specs, check_vma=False
    )
```

```python
import jax
import jax.numpy as jnp
from jax import lax
from jax.sharding import Mesh
from jax.sharding import PartitionSpec as P

STEPS = 3


clip_low = 1e-05
high = lax.Precision.HIGHEST

IND_AXES = ("yh", "yl", "z")
SNP_AXES = ("x", "c")
ROW_GROUP = ("yl", "z")
COL_GROUP = ("c", "x", "yh")


def doubling_sum(value, axes):
    for name in axes:
        size = lax.axis_size(name)
        step = 1
        while step < size:
            pairs = [(j, j ^ step) for j in range(size)]
            value = value + lax.ppermute(value, name, pairs)
            step *= 2
    return value


def doubling_gather(value, axes):
    for name in reversed(axes):
        size = lax.axis_size(name)
        me = lax.axis_index(name)
        step = 1
        while step < size:
            pairs = [(j, j ^ step) for j in range(size)]
            other = lax.ppermute(value, name, pairs)
            upper = (me // step) % 2 == 1
            value = jnp.where(upper, jnp.concatenate([other, value]), jnp.concatenate([value, other]))
            step *= 2
    return value


def per_device(genotypes, observed, ancestry, freqs):
    quarter = lax.axis_size("yh")
    geno = genotypes.astype(jnp.float32)
    seen = observed.astype(jnp.float32)
    counts = jnp.stack([seen * geno, seen * (2.0 - geno)])
    counts = lax.all_to_all(counts, "yh", 2, 1, tiled=True)
    hits, misses = counts[0], counts[1]
    own_rows = ancestry.shape[0]
    own_snps = freqs.shape[0]
    q_own = ancestry / jnp.sum(ancestry, axis=1, keepdims=True)
    q_zero = doubling_gather(q_own, ("yh",))
    f_zero = doubling_gather(freqs, ROW_GROUP)

    def em_map(q_rows, f_state):
        prob = jnp.dot(q_rows, f_state.T, precision=high, preferred_element_type=jnp.float32)
        ratio_a = hits / prob
        ratio_b = misses / (1.0 - prob)
        sum_a = jnp.dot(ratio_a, f_state, precision=high, preferred_element_type=jnp.float32)
        sum_b = jnp.dot(ratio_b, 1.0 - f_state, precision=high, preferred_element_type=jnp.float32)
        c_part = lax.dot_general(
            ratio_a, q_rows, (((0,), (0,)), ((), ())), precision=high, preferred_element_type=jnp.float32
        )
        d_part = lax.dot_general(
            ratio_b, q_rows, (((0,), (0,)), ((), ())), precision=high, preferred_element_type=jnp.float32
        )
        q_sum = doubling_sum(sum_a + sum_b, COL_GROUP)
        cd_total = doubling_sum(jnp.concatenate([c_part, d_part], axis=1), ROW_GROUP)
        q_next = q_rows * q_sum
        q_next = q_next / jnp.sum(q_next, axis=1, keepdims=True)
        width = f_state.shape[1]
        c_total, d_total = cd_total[:, :width], cd_total[:, width:]
        f_next = f_state * c_total / (f_state * c_total + (1.0 - f_state) * d_total)
        return (q_next, f_next)

    for step in range(STEPS):
        q_one, f_one = em_map(q_zero, f_zero)
        q_two, f_two = em_map(q_one, f_one)
        rq = q_one - q_zero
        rf = f_one - f_zero
        vq = q_two - 2.0 * q_one + q_zero
        vf = f_two - 2.0 * f_one + f_zero
        q_parts = doubling_sum(jnp.stack([jnp.sum(rq * rq), jnp.sum(vq * vq)]), ROW_GROUP)
        f_parts = doubling_sum(jnp.stack([jnp.sum(rf * rf), jnp.sum(vf * vf)]), COL_GROUP)
        first = q_parts[0] + f_parts[0]
        second = q_parts[1] + f_parts[1]
        alpha = -jnp.sqrt(first / (second + 1e-20))
        q_ext = jnp.clip(q_zero - 2.0 * alpha * rq + alpha * alpha * vq, clip_low, 1.0 - clip_low)
        q_zero = q_ext / jnp.sum(q_ext, axis=1, keepdims=True)
        f_zero = jnp.clip(f_zero - 2.0 * alpha * rf + alpha * alpha * vf, clip_low, 1.0 - clip_low)
    q_final = lax.dynamic_slice_in_dim(q_zero, lax.axis_index("yh") * own_rows, own_rows, 0)
    f_index = lax.axis_index("yl") * lax.axis_size("z") + lax.axis_index("z")
    f_final = lax.dynamic_slice_in_dim(f_zero, f_index * own_snps, own_snps, 0)
    del quarter
    return (q_final, f_final)


def solution(mesh):
    ind_size = mesh.shape["ind"]
    snp_size = mesh.shape["snp"]
    quarter = 4
    lanes = ind_size // quarter
    view = Mesh(
        mesh.devices.reshape(quarter, 2, lanes // 2, snp_size // 2, 2),
        ("yh", "yl", "z", "x", "c"),
    )
    in_specs = (
        P(IND_AXES, SNP_AXES),
        P(IND_AXES, SNP_AXES),
        P(IND_AXES, None),
        P(SNP_AXES + IND_AXES, None),
    )
    out_specs = (P(IND_AXES, None), P(SNP_AXES + IND_AXES, None))
    return jax.shard_map(
        per_device, mesh=view, in_specs=in_specs, out_specs=out_specs, check_vma=False
    )
```

```python
import jax
import jax.numpy as jnp
from jax import lax
from jax.sharding import Mesh
from jax.sharding import PartitionSpec as P

STEPS = 3


clip_low = 1e-05
high = lax.Precision.HIGHEST

IND_AXES = ("yh", "yl", "z")
SNP_AXES = ("x", "c")
ROW_GROUP = ("yl", "z")
COL_GROUP = ("c", "x", "yh")


def doubling_sum(value, axes):
    for name in axes:
        size = lax.axis_size(name)
        step = 1
        while step < size:
            pairs = [(j, j ^ step) for j in range(size)]
            value = value + lax.ppermute(value, name, pairs)
            step *= 2
    return value


def group_total(value, axes):
    count = 1
    for name in axes:
        count *= lax.axis_size(name)
    spread = jnp.broadcast_to(value[None], (count,) + value.shape)
    gathered = lax.all_to_all(spread, axes, 0, 0, tiled=True)
    return jnp.sum(gathered, axis=0)


def doubling_gather(value, axes):
    for name in reversed(axes):
        size = lax.axis_size(name)
        me = lax.axis_index(name)
        step = 1
        while step < size:
            pairs = [(j, j ^ step) for j in range(size)]
            other = lax.ppermute(value, name, pairs)
            upper = (me // step) % 2 == 1
            value = jnp.where(upper, jnp.concatenate([other, value]), jnp.concatenate([value, other]))
            step *= 2
    return value


def per_device(genotypes, observed, ancestry, freqs):
    quarter = lax.axis_size("yh")
    geno = genotypes.astype(jnp.float32)
    seen = observed.astype(jnp.float32)
    counts = jnp.stack([seen * geno, seen * (2.0 - geno)])
    counts = lax.all_to_all(counts, "yh", 2, 1, tiled=True)
    hits, misses = counts[0], counts[1]
    own_rows = ancestry.shape[0]
    own_snps = freqs.shape[0]
    q_own = ancestry / jnp.sum(ancestry, axis=1, keepdims=True)
    q_zero = doubling_gather(q_own, ("yh",))
    f_zero = doubling_gather(freqs, ROW_GROUP)

    def em_map(q_rows, f_state):
        prob = jnp.dot(q_rows, f_state.T, precision=high, preferred_element_type=jnp.float32)
        ratio_a = hits / prob
        ratio_b = misses / (1.0 - prob)
        sum_a = jnp.dot(ratio_a, f_state, precision=high, preferred_element_type=jnp.float32)
        sum_b = jnp.dot(ratio_b, 1.0 - f_state, precision=high, preferred_element_type=jnp.float32)
        c_part = lax.dot_general(
            ratio_a, q_rows, (((0,), (0,)), ((), ())), precision=high, preferred_element_type=jnp.float32
        )
        d_part = lax.dot_general(
            ratio_b, q_rows, (((0,), (0,)), ((), ())), precision=high, preferred_element_type=jnp.float32
        )
        q_sum = doubling_sum(sum_a + sum_b, COL_GROUP)
        cd_total = doubling_sum(jnp.concatenate([c_part, d_part], axis=1), ROW_GROUP)
        q_next = q_rows * q_sum
        q_next = q_next / jnp.sum(q_next, axis=1, keepdims=True)
        width = f_state.shape[1]
        c_total, d_total = cd_total[:, :width], cd_total[:, width:]
        f_next = f_state * c_total / (f_state * c_total + (1.0 - f_state) * d_total)
        return (q_next, f_next)

    for step in range(STEPS):
        q_one, f_one = em_map(q_zero, f_zero)
        q_two, f_two = em_map(q_one, f_one)
        rq = q_one - q_zero
        rf = f_one - f_zero
        vq = q_two - 2.0 * q_one + q_zero
        vf = f_two - 2.0 * f_one + f_zero
        q_parts = group_total(jnp.stack([jnp.sum(rq * rq), jnp.sum(vq * vq)]), ROW_GROUP)
        f_parts = group_total(jnp.stack([jnp.sum(rf * rf), jnp.sum(vf * vf)]), COL_GROUP)
        first = q_parts[0] + f_parts[0]
        second = q_parts[1] + f_parts[1]
        alpha = -jnp.sqrt(first / (second + 1e-20))
        q_ext = jnp.clip(q_zero - 2.0 * alpha * rq + alpha * alpha * vq, clip_low, 1.0 - clip_low)
        q_zero = q_ext / jnp.sum(q_ext, axis=1, keepdims=True)
        f_zero = jnp.clip(f_zero - 2.0 * alpha * rf + alpha * alpha * vf, clip_low, 1.0 - clip_low)
    q_final = lax.dynamic_slice_in_dim(q_zero, lax.axis_index("yh") * own_rows, own_rows, 0)
    f_index = lax.axis_index("yl") * lax.axis_size("z") + lax.axis_index("z")
    f_final = lax.dynamic_slice_in_dim(f_zero, f_index * own_snps, own_snps, 0)
    del quarter
    return (q_final, f_final)


def solution(mesh):
    ind_size = mesh.shape["ind"]
    snp_size = mesh.shape["snp"]
    quarter = 4
    lanes = ind_size // quarter
    view = Mesh(
        mesh.devices.reshape(quarter, 2, lanes // 2, snp_size // 2, 2),
        ("yh", "yl", "z", "x", "c"),
    )
    in_specs = (
        P(IND_AXES, SNP_AXES),
        P(IND_AXES, SNP_AXES),
        P(IND_AXES, None),
        P(SNP_AXES + IND_AXES, None),
    )
    out_specs = (P(IND_AXES, None), P(SNP_AXES + IND_AXES, None))
    return jax.shard_map(
        per_device, mesh=view, in_specs=in_specs, out_specs=out_specs, check_vma=False
    )
```

```python
import jax
import jax.numpy as jnp
from jax import lax
from jax.sharding import Mesh
from jax.sharding import PartitionSpec as P

STEPS = 3


clip_low = 1e-05
high = lax.Precision.HIGHEST

IND_AXES = ("yh", "yl", "z")
SNP_AXES = ("x", "c")
ROW_GROUP = ("yl", "z")
COL_GROUP = ("c", "x", "yh")


def doubling_sum(value, axes):
    for name in axes:
        size = lax.axis_size(name)
        step = 1
        while step < size:
            pairs = [(j, j ^ step) for j in range(size)]
            value = value + lax.ppermute(value, name, pairs)
            step *= 2
    return value


def group_total(value, axes):
    count = 1
    for name in axes:
        count *= lax.axis_size(name)
    spread = jnp.broadcast_to(value[None], (count,) + value.shape)
    gathered = lax.all_to_all(spread, axes, 0, 0, tiled=True)
    return jnp.sum(gathered, axis=0)


def doubling_gather(value, axes):
    for name in reversed(axes):
        size = lax.axis_size(name)
        me = lax.axis_index(name)
        step = 1
        while step < size:
            pairs = [(j, j ^ step) for j in range(size)]
            other = lax.ppermute(value, name, pairs)
            upper = (me // step) % 2 == 1
            value = jnp.where(upper, jnp.concatenate([other, value]), jnp.concatenate([value, other]))
            step *= 2
    return value


def per_device(genotypes, observed, ancestry, freqs):
    quarter = lax.axis_size("yh")
    geno = genotypes.astype(jnp.float32)
    seen = observed.astype(jnp.float32)
    counts = jnp.stack([seen * geno, seen * (2.0 - geno)])
    counts = lax.all_to_all(counts, "yh", 2, 1, tiled=True)
    hits, misses = counts[0], counts[1]
    own_rows = ancestry.shape[0]
    own_snps = freqs.shape[0]
    q_own = ancestry / jnp.sum(ancestry, axis=1, keepdims=True)
    q_zero = doubling_gather(q_own, ("yh",))
    f_zero = doubling_gather(freqs, ROW_GROUP)

    def em_map(q_rows, f_state):
        prob = jnp.dot(q_rows, f_state.T, precision=high, preferred_element_type=jnp.float32)
        ratio_a = hits / prob
        ratio_b = misses / (1.0 - prob)
        sum_a = jnp.dot(ratio_a, f_state, precision=high, preferred_element_type=jnp.float32)
        sum_b = jnp.dot(ratio_b, 1.0 - f_state, precision=high, preferred_element_type=jnp.float32)
        c_part = lax.dot_general(
            ratio_a, q_rows, (((0,), (0,)), ((), ())), precision=high, preferred_element_type=jnp.float32
        )
        d_part = lax.dot_general(
            ratio_b, q_rows, (((0,), (0,)), ((), ())), precision=high, preferred_element_type=jnp.float32
        )
        q_sum = doubling_sum(sum_a + sum_b, COL_GROUP)
        cd_total = doubling_sum(jnp.concatenate([c_part, d_part], axis=1), ROW_GROUP)
        q_next = q_rows * q_sum
        q_next = q_next / jnp.sum(q_next, axis=1, keepdims=True)
        width = f_state.shape[1]
        c_total, d_total = cd_total[:, :width], cd_total[:, width:]
        f_next = f_state * c_total / (f_state * c_total + (1.0 - f_state) * d_total)
        return (q_next, f_next)

    def one_step(step, state):
        q_zero, f_zero = state
        q_one, f_one = em_map(q_zero, f_zero)
        q_two, f_two = em_map(q_one, f_one)
        rq = q_one - q_zero
        rf = f_one - f_zero
        vq = q_two - 2.0 * q_one + q_zero
        vf = f_two - 2.0 * f_one + f_zero
        q_parts = group_total(jnp.stack([jnp.sum(rq * rq), jnp.sum(vq * vq)]), ROW_GROUP)
        f_parts = group_total(jnp.stack([jnp.sum(rf * rf), jnp.sum(vf * vf)]), COL_GROUP)
        first = q_parts[0] + f_parts[0]
        second = q_parts[1] + f_parts[1]
        alpha = -jnp.sqrt(first / (second + 1e-20))
        q_ext = jnp.clip(q_zero - 2.0 * alpha * rq + alpha * alpha * vq, clip_low, 1.0 - clip_low)
        q_zero = q_ext / jnp.sum(q_ext, axis=1, keepdims=True)
        f_zero = jnp.clip(f_zero - 2.0 * alpha * rf + alpha * alpha * vf, clip_low, 1.0 - clip_low)
        return (q_zero, f_zero)

    q_zero, f_zero = lax.fori_loop(0, STEPS, one_step, (q_zero, f_zero))
    q_final = lax.dynamic_slice_in_dim(q_zero, lax.axis_index("yh") * own_rows, own_rows, 0)
    f_index = lax.axis_index("yl") * lax.axis_size("z") + lax.axis_index("z")
    f_final = lax.dynamic_slice_in_dim(f_zero, f_index * own_snps, own_snps, 0)
    del quarter
    return (q_final, f_final)


def solution(mesh):
    ind_size = mesh.shape["ind"]
    snp_size = mesh.shape["snp"]
    quarter = 4
    lanes = ind_size // quarter
    view = Mesh(
        mesh.devices.reshape(quarter, 2, lanes // 2, snp_size // 2, 2),
        ("yh", "yl", "z", "x", "c"),
    )
    in_specs = (
        P(IND_AXES, SNP_AXES),
        P(IND_AXES, SNP_AXES),
        P(IND_AXES, None),
        P(SNP_AXES + IND_AXES, None),
    )
    out_specs = (P(IND_AXES, None), P(SNP_AXES + IND_AXES, None))
    return jax.shard_map(
        per_device, mesh=view, in_specs=in_specs, out_specs=out_specs, check_vma=False
    )
```

```python
import jax
import jax.numpy as jnp
from jax import lax
from jax.sharding import Mesh
from jax.sharding import PartitionSpec as P

STEPS = 3


clip_low = 1e-05
high = lax.Precision.HIGHEST

IND_AXES = ("yh", "yl", "z")
SNP_AXES = ("x", "c")
ROW_GROUP = ("yl", "z")
COL_GROUP = ("c", "x", "yh")


def doubling_sum(value, axes):
    for name in axes:
        size = lax.axis_size(name)
        step = 1
        while step < size:
            pairs = [(j, j ^ step) for j in range(size)]
            value = value + lax.ppermute(value, name, pairs)
            step *= 2
    return value


def group_total(value, axes):
    count = 1
    for name in axes:
        count *= lax.axis_size(name)
    spread = jnp.broadcast_to(value[None], (count,) + value.shape)
    gathered = lax.all_to_all(spread, axes, 0, 0, tiled=True)
    return jnp.sum(gathered, axis=0)


def exchange_sum(value, axes):
    count = 1
    for name in axes:
        count *= lax.axis_size(name)
    chunks = value.reshape((count, value.shape[0] // count) + value.shape[1:])
    owned = jnp.sum(lax.all_to_all(chunks, axes, 0, 0, tiled=True), axis=0)
    spread = jnp.broadcast_to(owned[None], chunks.shape)
    return lax.all_to_all(spread, axes, 0, 0, tiled=True).reshape(value.shape)


def doubling_gather(value, axes):
    for name in reversed(axes):
        size = lax.axis_size(name)
        me = lax.axis_index(name)
        step = 1
        while step < size:
            pairs = [(j, j ^ step) for j in range(size)]
            other = lax.ppermute(value, name, pairs)
            upper = (me // step) % 2 == 1
            value = jnp.where(upper, jnp.concatenate([other, value]), jnp.concatenate([value, other]))
            step *= 2
    return value


def per_device(genotypes, observed, ancestry, freqs):
    quarter = lax.axis_size("yh")
    geno = genotypes.astype(jnp.float32)
    seen = observed.astype(jnp.float32)
    counts = jnp.stack([seen * geno, seen * (2.0 - geno)])
    counts = lax.all_to_all(counts, "yh", 2, 1, tiled=True)
    hits, misses = counts[0], counts[1]
    own_rows = ancestry.shape[0]
    own_snps = freqs.shape[0]
    q_own = ancestry / jnp.sum(ancestry, axis=1, keepdims=True)
    q_zero = doubling_gather(q_own, ("yh",))
    f_zero = doubling_gather(freqs, ROW_GROUP)

    def em_map(q_rows, f_state):
        prob = jnp.dot(q_rows, f_state.T, precision=high, preferred_element_type=jnp.float32)
        ratio_a = hits / prob
        ratio_b = misses / (1.0 - prob)
        sum_a = jnp.dot(ratio_a, f_state, precision=high, preferred_element_type=jnp.float32)
        sum_b = jnp.dot(ratio_b, 1.0 - f_state, precision=high, preferred_element_type=jnp.float32)
        c_part = lax.dot_general(
            ratio_a, q_rows, (((0,), (0,)), ((), ())), precision=high, preferred_element_type=jnp.float32
        )
        d_part = lax.dot_general(
            ratio_b, q_rows, (((0,), (0,)), ((), ())), precision=high, preferred_element_type=jnp.float32
        )
        q_sum = doubling_sum(sum_a + sum_b, COL_GROUP)
        cd_total = exchange_sum(jnp.concatenate([c_part, d_part], axis=1), ROW_GROUP)
        q_next = q_rows * q_sum
        q_next = q_next / jnp.sum(q_next, axis=1, keepdims=True)
        width = f_state.shape[1]
        c_total, d_total = cd_total[:, :width], cd_total[:, width:]
        f_next = f_state * c_total / (f_state * c_total + (1.0 - f_state) * d_total)
        return (q_next, f_next)

    for step in range(STEPS):
        q_one, f_one = em_map(q_zero, f_zero)
        q_two, f_two = em_map(q_one, f_one)
        rq = q_one - q_zero
        rf = f_one - f_zero
        vq = q_two - 2.0 * q_one + q_zero
        vf = f_two - 2.0 * f_one + f_zero
        q_parts = group_total(jnp.stack([jnp.sum(rq * rq), jnp.sum(vq * vq)]), ROW_GROUP)
        f_parts = group_total(jnp.stack([jnp.sum(rf * rf), jnp.sum(vf * vf)]), COL_GROUP)
        first = q_parts[0] + f_parts[0]
        second = q_parts[1] + f_parts[1]
        alpha = -jnp.sqrt(first / (second + 1e-20))
        q_ext = jnp.clip(q_zero - 2.0 * alpha * rq + alpha * alpha * vq, clip_low, 1.0 - clip_low)
        q_zero = q_ext / jnp.sum(q_ext, axis=1, keepdims=True)
        f_zero = jnp.clip(f_zero - 2.0 * alpha * rf + alpha * alpha * vf, clip_low, 1.0 - clip_low)
    q_final = lax.dynamic_slice_in_dim(q_zero, lax.axis_index("yh") * own_rows, own_rows, 0)
    f_index = lax.axis_index("yl") * lax.axis_size("z") + lax.axis_index("z")
    f_final = lax.dynamic_slice_in_dim(f_zero, f_index * own_snps, own_snps, 0)
    del quarter
    return (q_final, f_final)


def solution(mesh):
    ind_size = mesh.shape["ind"]
    snp_size = mesh.shape["snp"]
    quarter = 4
    lanes = ind_size // quarter
    view = Mesh(
        mesh.devices.reshape(quarter, 2, lanes // 2, snp_size // 2, 2),
        ("yh", "yl", "z", "x", "c"),
    )
    in_specs = (
        P(IND_AXES, SNP_AXES),
        P(IND_AXES, SNP_AXES),
        P(IND_AXES, None),
        P(SNP_AXES + IND_AXES, None),
    )
    out_specs = (P(IND_AXES, None), P(SNP_AXES + IND_AXES, None))
    return jax.shard_map(
        per_device, mesh=view, in_specs=in_specs, out_specs=out_specs, check_vma=False
    )
```

```python
import jax
import jax.numpy as jnp
from jax import lax
from jax.sharding import Mesh
from jax.sharding import PartitionSpec as P

STEPS = 3


clip_low = 1e-05
high = lax.Precision.HIGHEST

IND_AXES = ("yh", "yl", "z")
SNP_AXES = ("x", "c")
ROW_GROUP = ("yl", "z")
COL_GROUP = ("c", "x", "yh")


def doubling_sum(value, axes):
    for name in axes:
        size = lax.axis_size(name)
        step = 1
        while step < size:
            pairs = [(j, j ^ step) for j in range(size)]
            value = value + lax.ppermute(value, name, pairs)
            step *= 2
    return value


def group_total(value, axes):
    count = 1
    for name in axes:
        count *= lax.axis_size(name)
    spread = jnp.broadcast_to(value[None], (count,) + value.shape)
    gathered = lax.all_to_all(spread, axes, 0, 0, tiled=True)
    return jnp.sum(gathered, axis=0)


def doubling_gather(value, axes):
    for name in reversed(axes):
        size = lax.axis_size(name)
        me = lax.axis_index(name)
        step = 1
        while step < size:
            pairs = [(j, j ^ step) for j in range(size)]
            other = lax.ppermute(value, name, pairs)
            upper = (me // step) % 2 == 1
            value = jnp.where(upper, jnp.concatenate([other, value]), jnp.concatenate([value, other]))
            step *= 2
    return value


def per_device(genotypes, observed, ancestry, freqs):
    quarter = lax.axis_size("yh")
    rows, width = genotypes.shape
    geno = genotypes.astype(jnp.float32).reshape(rows, quarter, width // quarter).transpose(1, 0, 2)
    seen = observed.astype(jnp.float32).reshape(rows, quarter, width // quarter).transpose(1, 0, 2)
    counts = jnp.stack([seen * geno, seen * (2.0 - geno)], axis=1)
    counts = lax.all_to_all(counts, "yh", 0, 0, tiled=True)
    hits = counts[:, 0].reshape(quarter * rows, width // quarter)
    misses = counts[:, 1].reshape(quarter * rows, width // quarter)
    own_rows = ancestry.shape[0]
    own_snps = freqs.shape[0]
    q_own = ancestry / jnp.sum(ancestry, axis=1, keepdims=True)
    q_zero = doubling_gather(q_own, ("yh",))
    f_zero = doubling_gather(freqs, ROW_GROUP)

    def em_map(q_rows, f_state):
        prob = jnp.dot(q_rows, f_state.T, precision=high, preferred_element_type=jnp.float32)
        ratio_a = hits / prob
        ratio_b = misses / (1.0 - prob)
        sum_a = jnp.dot(ratio_a, f_state, precision=high, preferred_element_type=jnp.float32)
        sum_b = jnp.dot(ratio_b, 1.0 - f_state, precision=high, preferred_element_type=jnp.float32)
        c_part = lax.dot_general(
            ratio_a, q_rows, (((0,), (0,)), ((), ())), precision=high, preferred_element_type=jnp.float32
        )
        d_part = lax.dot_general(
            ratio_b, q_rows, (((0,), (0,)), ((), ())), precision=high, preferred_element_type=jnp.float32
        )
        q_sum = doubling_sum(sum_a + sum_b, COL_GROUP)
        cd_total = doubling_sum(jnp.concatenate([c_part, d_part], axis=1), ROW_GROUP)
        q_next = q_rows * q_sum
        q_next = q_next / jnp.sum(q_next, axis=1, keepdims=True)
        width = f_state.shape[1]
        c_total, d_total = cd_total[:, :width], cd_total[:, width:]
        f_next = f_state * c_total / (f_state * c_total + (1.0 - f_state) * d_total)
        return (q_next, f_next)

    for step in range(STEPS):
        q_one, f_one = em_map(q_zero, f_zero)
        q_two, f_two = em_map(q_one, f_one)
        rq = q_one - q_zero
        rf = f_one - f_zero
        vq = q_two - 2.0 * q_one + q_zero
        vf = f_two - 2.0 * f_one + f_zero
        q_parts = group_total(jnp.stack([jnp.sum(rq * rq), jnp.sum(vq * vq)]), ROW_GROUP)
        f_parts = group_total(jnp.stack([jnp.sum(rf * rf), jnp.sum(vf * vf)]), COL_GROUP)
        first = q_parts[0] + f_parts[0]
        second = q_parts[1] + f_parts[1]
        alpha = -jnp.sqrt(first / (second + 1e-20))
        q_ext = jnp.clip(q_zero - 2.0 * alpha * rq + alpha * alpha * vq, clip_low, 1.0 - clip_low)
        q_zero = q_ext / jnp.sum(q_ext, axis=1, keepdims=True)
        f_zero = jnp.clip(f_zero - 2.0 * alpha * rf + alpha * alpha * vf, clip_low, 1.0 - clip_low)
    q_final = lax.dynamic_slice_in_dim(q_zero, lax.axis_index("yh") * own_rows, own_rows, 0)
    f_index = lax.axis_index("yl") * lax.axis_size("z") + lax.axis_index("z")
    f_final = lax.dynamic_slice_in_dim(f_zero, f_index * own_snps, own_snps, 0)
    return (q_final, f_final)


def solution(mesh):
    ind_size = mesh.shape["ind"]
    snp_size = mesh.shape["snp"]
    quarter = 4
    lanes = ind_size // quarter
    view = Mesh(
        mesh.devices.reshape(quarter, 2, lanes // 2, snp_size // 2, 2),
        ("yh", "yl", "z", "x", "c"),
    )
    in_specs = (
        P(IND_AXES, SNP_AXES),
        P(IND_AXES, SNP_AXES),
        P(IND_AXES, None),
        P(SNP_AXES + IND_AXES, None),
    )
    out_specs = (P(IND_AXES, None), P(SNP_AXES + IND_AXES, None))
    return jax.shard_map(
        per_device, mesh=view, in_specs=in_specs, out_specs=out_specs, check_vma=False
    )
```

```python
import jax
import jax.numpy as jnp
from jax import lax
from jax.sharding import Mesh
from jax.sharding import PartitionSpec as P

STEPS = 3


clip_low = 1e-05
high = lax.Precision.HIGHEST

IND_AXES = ("yh", "yl", "z")
SNP_AXES = ("x", "c")
ROW_GROUP = ("yl", "z")
COL_GROUP = ("c", "x", "yh")


def doubling_sum(value, axes):
    for name in axes:
        size = lax.axis_size(name)
        step = 1
        while step < size:
            pairs = [(j, j ^ step) for j in range(size)]
            value = value + lax.ppermute(value, name, pairs)
            step *= 2
    return value


def group_total(value, axes):
    count = 1
    for name in axes:
        count *= lax.axis_size(name)
    spread = jnp.broadcast_to(value[None], (count,) + value.shape)
    gathered = lax.all_to_all(spread, axes, 0, 0, tiled=True)
    return jnp.sum(gathered, axis=0)


def doubling_gather(value, axes):
    for name in reversed(axes):
        size = lax.axis_size(name)
        me = lax.axis_index(name)
        step = 1
        while step < size:
            pairs = [(j, j ^ step) for j in range(size)]
            other = lax.ppermute(value, name, pairs)
            upper = (me // step) % 2 == 1
            value = jnp.where(upper, jnp.concatenate([other, value]), jnp.concatenate([value, other]))
            step *= 2
    return value


def per_device(genotypes, observed, ancestry, freqs):
    quarter = lax.axis_size("yh")
    rows, width = genotypes.shape
    geno = genotypes.astype(jnp.float32).reshape(rows, quarter, width // quarter).transpose(1, 0, 2)
    seen = observed.astype(jnp.float32).reshape(rows, quarter, width // quarter).transpose(1, 0, 2)
    counts = jnp.stack([seen * geno, seen * (2.0 - geno)], axis=1)
    me = lax.axis_index("yh")
    arrived = [lax.dynamic_index_in_dim(counts, me, 0, keepdims=False)]
    for shift in range(1, quarter):
        outgoing = lax.dynamic_index_in_dim(counts, (me + shift) % quarter, 0, keepdims=False)
        pairs = [(j, (j + shift) % quarter) for j in range(quarter)]
        arrived.append(lax.ppermute(outgoing, "yh", pairs))
    arrived = jnp.stack(arrived)
    counts = jnp.stack(
        [lax.dynamic_index_in_dim(arrived, (me - src) % quarter, 0, keepdims=False) for src in range(quarter)]
    )
    hits = counts[:, 0].reshape(quarter * rows, width // quarter)
    misses = counts[:, 1].reshape(quarter * rows, width // quarter)
    own_rows = ancestry.shape[0]
    own_snps = freqs.shape[0]
    q_own = ancestry / jnp.sum(ancestry, axis=1, keepdims=True)
    q_zero = doubling_gather(q_own, ("yh",))
    f_zero = doubling_gather(freqs, ROW_GROUP)

    def em_map(q_rows, f_state):
        prob = jnp.dot(q_rows, f_state.T, precision=high, preferred_element_type=jnp.float32)
        ratio_a = hits / prob
        ratio_b = misses / (1.0 - prob)
        sum_a = jnp.dot(ratio_a, f_state, precision=high, preferred_element_type=jnp.float32)
        sum_b = jnp.dot(ratio_b, 1.0 - f_state, precision=high, preferred_element_type=jnp.float32)
        c_part = lax.dot_general(
            ratio_a, q_rows, (((0,), (0,)), ((), ())), precision=high, preferred_element_type=jnp.float32
        )
        d_part = lax.dot_general(
            ratio_b, q_rows, (((0,), (0,)), ((), ())), precision=high, preferred_element_type=jnp.float32
        )
        q_sum = doubling_sum(sum_a + sum_b, COL_GROUP)
        cd_total = doubling_sum(jnp.concatenate([c_part, d_part], axis=1), ROW_GROUP)
        q_next = q_rows * q_sum
        q_next = q_next / jnp.sum(q_next, axis=1, keepdims=True)
        width = f_state.shape[1]
        c_total, d_total = cd_total[:, :width], cd_total[:, width:]
        f_next = f_state * c_total / (f_state * c_total + (1.0 - f_state) * d_total)
        return (q_next, f_next)

    for step in range(STEPS):
        q_one, f_one = em_map(q_zero, f_zero)
        q_two, f_two = em_map(q_one, f_one)
        rq = q_one - q_zero
        rf = f_one - f_zero
        vq = q_two - 2.0 * q_one + q_zero
        vf = f_two - 2.0 * f_one + f_zero
        q_parts = group_total(jnp.stack([jnp.sum(rq * rq), jnp.sum(vq * vq)]), ROW_GROUP)
        f_parts = group_total(jnp.stack([jnp.sum(rf * rf), jnp.sum(vf * vf)]), COL_GROUP)
        first = q_parts[0] + f_parts[0]
        second = q_parts[1] + f_parts[1]
        alpha = -jnp.sqrt(first / (second + 1e-20))
        q_ext = jnp.clip(q_zero - 2.0 * alpha * rq + alpha * alpha * vq, clip_low, 1.0 - clip_low)
        q_zero = q_ext / jnp.sum(q_ext, axis=1, keepdims=True)
        f_zero = jnp.clip(f_zero - 2.0 * alpha * rf + alpha * alpha * vf, clip_low, 1.0 - clip_low)
    q_final = lax.dynamic_slice_in_dim(q_zero, lax.axis_index("yh") * own_rows, own_rows, 0)
    f_index = lax.axis_index("yl") * lax.axis_size("z") + lax.axis_index("z")
    f_final = lax.dynamic_slice_in_dim(f_zero, f_index * own_snps, own_snps, 0)
    return (q_final, f_final)


def solution(mesh):
    ind_size = mesh.shape["ind"]
    snp_size = mesh.shape["snp"]
    quarter = 4
    lanes = ind_size // quarter
    view = Mesh(
        mesh.devices.reshape(quarter, 2, lanes // 2, snp_size // 2, 2),
        ("yh", "yl", "z", "x", "c"),
    )
    in_specs = (
        P(IND_AXES, SNP_AXES),
        P(IND_AXES, SNP_AXES),
        P(IND_AXES, None),
        P(SNP_AXES + IND_AXES, None),
    )
    out_specs = (P(IND_AXES, None), P(SNP_AXES + IND_AXES, None))
    return jax.shard_map(
        per_device, mesh=view, in_specs=in_specs, out_specs=out_specs, check_vma=False
    )
```

```python
import jax
import jax.numpy as jnp
from jax import lax
from jax.sharding import Mesh
from jax.sharding import PartitionSpec as P

STEPS = 3


clip_low = 1e-05
high = lax.Precision.HIGHEST

IND_AXES = ("yh", "yl", "z")
SNP_AXES = ("x", "c")
ROW_GROUP = ("yl", "z")
COL_GROUP = ("c", "x", "yh")


def doubling_sum(value, axes):
    for name in axes:
        size = lax.axis_size(name)
        step = 1
        while step < size:
            pairs = [(j, j ^ step) for j in range(size)]
            value = value + lax.ppermute(value, name, pairs)
            step *= 2
    return value


def group_total(value, axes):
    count = 1
    for name in axes:
        count *= lax.axis_size(name)
    spread = jnp.broadcast_to(value[None], (count,) + value.shape)
    gathered = lax.all_to_all(spread, axes, 0, 0, tiled=True)
    return jnp.sum(gathered, axis=0)


def doubling_gather(value, axes):
    for name in reversed(axes):
        size = lax.axis_size(name)
        me = lax.axis_index(name)
        step = 1
        while step < size:
            pairs = [(j, j ^ step) for j in range(size)]
            other = lax.ppermute(value, name, pairs)
            upper = (me // step) % 2 == 1
            value = jnp.where(upper, jnp.concatenate([other, value]), jnp.concatenate([value, other]))
            step *= 2
    return value


def per_device(genotypes, observed, ancestry, freqs):
    quarter = lax.axis_size("yh")
    rows, width = genotypes.shape
    geno = genotypes.astype(jnp.float32).reshape(rows, quarter, width // quarter).transpose(1, 0, 2)
    seen = observed.astype(jnp.float32).reshape(rows, quarter, width // quarter).transpose(1, 0, 2)
    counts = jnp.stack([seen * geno, seen * (2.0 - geno)], axis=1)
    counts = lax.all_to_all(counts, "yh", 0, 0, tiled=True)
    hits = counts[:, 0].reshape(quarter * rows, width // quarter)
    misses = counts[:, 1].reshape(quarter * rows, width // quarter)
    own_rows = ancestry.shape[0]
    own_snps = freqs.shape[0]
    q_own = ancestry / jnp.sum(ancestry, axis=1, keepdims=True)
    q_zero = doubling_gather(q_own, ("yh",))
    f_zero = doubling_gather(freqs, ROW_GROUP)

    def em_map(q_rows, f_state):
        prob = jnp.dot(q_rows, f_state.T, precision=high, preferred_element_type=jnp.float32)
        ratio_a = hits / prob
        ratio_b = misses / (1.0 - prob)
        sum_a = jnp.dot(ratio_a, f_state, precision=high, preferred_element_type=jnp.float32)
        sum_b = jnp.dot(ratio_b, 1.0 - f_state, precision=high, preferred_element_type=jnp.float32)
        c_part = lax.dot_general(
            ratio_a, q_rows, (((0,), (0,)), ((), ())), precision=high, preferred_element_type=jnp.float32
        )
        d_part = lax.dot_general(
            ratio_b, q_rows, (((0,), (0,)), ((), ())), precision=high, preferred_element_type=jnp.float32
        )
        q_sum = doubling_sum(sum_a + sum_b, COL_GROUP)
        cd_total = doubling_sum(jnp.concatenate([c_part, d_part], axis=1), ROW_GROUP)
        q_next = q_rows * q_sum
        q_next = q_next / jnp.sum(q_next, axis=1, keepdims=True)
        width = f_state.shape[1]
        c_total, d_total = cd_total[:, :width], cd_total[:, width:]
        f_next = f_state * c_total / (f_state * c_total + (1.0 - f_state) * d_total)
        return (q_next, f_next)

    for step in range(STEPS):
        q_one, f_one = em_map(q_zero, f_zero)
        q_two, f_two = em_map(q_one, f_one)
        rq = q_one - q_zero
        rf = f_one - f_zero
        vq = q_two - 2.0 * q_one + q_zero
        vf = f_two - 2.0 * f_one + f_zero
        q_parts = doubling_sum(jnp.stack([jnp.sum(rq * rq), jnp.sum(vq * vq)]), ROW_GROUP)
        f_parts = group_total(jnp.stack([jnp.sum(rf * rf), jnp.sum(vf * vf)]), COL_GROUP)
        first = q_parts[0] + f_parts[0]
        second = q_parts[1] + f_parts[1]
        alpha = -jnp.sqrt(first / (second + 1e-20))
        q_ext = jnp.clip(q_zero - 2.0 * alpha * rq + alpha * alpha * vq, clip_low, 1.0 - clip_low)
        q_zero = q_ext / jnp.sum(q_ext, axis=1, keepdims=True)
        f_zero = jnp.clip(f_zero - 2.0 * alpha * rf + alpha * alpha * vf, clip_low, 1.0 - clip_low)
    q_final = lax.dynamic_slice_in_dim(q_zero, lax.axis_index("yh") * own_rows, own_rows, 0)
    f_index = lax.axis_index("yl") * lax.axis_size("z") + lax.axis_index("z")
    f_final = lax.dynamic_slice_in_dim(f_zero, f_index * own_snps, own_snps, 0)
    return (q_final, f_final)


def solution(mesh):
    ind_size = mesh.shape["ind"]
    snp_size = mesh.shape["snp"]
    quarter = 4
    lanes = ind_size // quarter
    view = Mesh(
        mesh.devices.reshape(quarter, 2, lanes // 2, snp_size // 2, 2),
        ("yh", "yl", "z", "x", "c"),
    )
    in_specs = (
        P(IND_AXES, SNP_AXES),
        P(IND_AXES, SNP_AXES),
        P(IND_AXES, None),
        P(SNP_AXES + IND_AXES, None),
    )
    out_specs = (P(IND_AXES, None), P(SNP_AXES + IND_AXES, None))
    return jax.shard_map(
        per_device, mesh=view, in_specs=in_specs, out_specs=out_specs, check_vma=False
    )
```
